128 devices in a mesh: row: 8 (over z_hi, x), lmk: 8 (over z_lo, y), bw: 2 (over core).
Axes of the slice: x: 4, y: 4, z: 4 (z_hi: 2, z_lo: 2; z = z_hi * 2 + z_lo), core: 2. Of those that a mesh axis runs over, the one named last changes fastest.
Arguments:
- embeddings: bfloat16 [24576, 1024], P(('row', 'lmk')), may hold values from -6 to 6
- candidates: bfloat16 [131072, 1024], P(('row', 'lmk')), may hold values from -6 to 6
- block_owner: int32 [2], replicated, may hold values from 0 to 63, as said below
- landmark_picks: int32 [2, 2048], replicated, may hold values from 0 to 2047, each once within a row
- inverse_width: float32 [8], P('bw'), may hold values from 2 to 16
- mixture: float32 [8], P('bw'), may hold values from 0.05 to 0.25
- whitening: bfloat16 [4096, 4096], P(None, 'bw'), may hold values from -0.09375 to 0.09375
Outputs:
- features: bfloat16 [24576, 4096], P(('row', 'lmk'), 'bw')
The draws below stay inside these ranges and needn't reach their ends.
Inputs may be any that keep to these rules, and one draw needn't show every extreme that they name: `block_owner`: the 2 owners are different, and 63 is one of them. `landmark_picks`: each row is an ordering of 0 to 2047.
All inputs are finite; a program needn't handle non-finite values.
Results may differ from the reference program's by a relative error of at most 0.0055.
Values may be sent and summed in bfloat16 or wider, within the bound.
No kernel may reach another device: no remote copies, remote signals or barrier semaphores. Data moves between devices by JAX's collectives and lax.ppermute only.
A program may use at most 128 MiB of HBM per device.

```python
import math
import jax
import jax.numpy as jnp
from jax import lax

D = 1024
BLK = 2048
NBLK = 2
NBW = 8
R_DEV = 384
M = 4096
OWNERS = 64
ROWS = 24576
POOL = 131072


def draw_block_owner(key, part):
    first_key, second_key = jax.random.split(key)
    other = jax.random.randint(first_key, (), 0, OWNERS - 1)
    flipped = jax.random.randint(second_key, (), 0, 2)
    highest = jnp.int32(OWNERS - 1)
    leading = jnp.where(flipped == 1, highest, other)
    trailing = jnp.where(flipped == 1, other, highest)
    return jnp.stack([leading, trailing]).astype(jnp.int32)


def levels(own_key, extent, cuts, smallest, largest):
    def one(axis_at, shards_of):
        steps = jax.random.uniform(jax.random.fold_in(jax.random.fold_in(own_key, 6), axis_at), (shards_of,), jnp.float32, smallest / len(cuts), largest / len(cuts))
        return jnp.repeat(jnp.exp(steps), extent[axis_at] // shards_of).reshape((-1,) + (1,) * (len(extent) - axis_at - 1))

    factor_of = one(*cuts[0])
    for cut in cuts[1:]:
        factor_of = factor_of * one(*cut)
    return factor_of


def bell_draw(own_key, shape, width, reach, pieces=(), kind=jnp.bfloat16):
    drawn = width * jax.random.normal(own_key, shape, jnp.float32)
    if pieces:
        drawn = drawn * levels(own_key, shape, pieces, -0.22, 0.18)
    return jnp.clip(drawn, -reach, reach).astype(kind)


def setup_inputs(seed: int = 0) -> dict:
    streams_of = jax.random.split(jax.random.key(seed), 8)
    embeddings = bell_draw(streams_of[0], (ROWS, D), 1.0, 6.0, ((0, 64),))
    candidates = bell_draw(streams_of[1], (POOL, D), 1.0, 6.0, ((0, 64),))
    block_owner = draw_block_owner(jax.random.fold_in(streams_of[7], 71), 0)
    landmark_picks = jax.vmap(lambda own: jax.random.permutation(own, BLK))(jax.random.split(streams_of[3], NBLK)).reshape((NBLK, BLK)).astype(jnp.int32)
    inverse_width = jnp.clip(jnp.exp(math.log(16.0) - 2.0794415 * jax.random.uniform(streams_of[4], (NBW,), jnp.float32) ** levels(streams_of[4], (NBW,), ((0, 2),), -0.2, 0.2)), 2.0, 16.0)
    mixture = jnp.clip(jnp.exp(math.log(0.25) - 1.609438 * jax.random.uniform(streams_of[5], (NBW,), jnp.float32) ** levels(streams_of[5], (NBW,), ((0, 2),), -0.2, 0.2)), 0.05, 0.25)
    whitening = bell_draw(streams_of[6], (M, M), M ** -0.5, 0.09375, ((1, 2),))
    return {"embeddings": embeddings, "candidates": candidates, "block_owner": block_owner, "landmark_picks": landmark_picks, "inverse_width": inverse_width, "mixture": mixture, "whitening": whitening}


def normalize(matrix_rows):
    widened = matrix_rows.astype(jnp.float32)
    scale = lax.rsqrt(lax.optimization_barrier(jnp.sum(widened * widened, axis=-1, keepdims=True)) + 1e-06)
    return (widened * scale).astype(jnp.bfloat16)

def kernel_of(cosine, widths, weights):
    running = jnp.zeros(cosine.shape, jnp.float32)
    for which in range(widths.shape[0]):
        running = running + weights[which] * jnp.exp(2.0 * widths[which] * cosine)
    return running

def reference(embeddings, candidates, block_owner, landmark_picks, inverse_width, mixture, whitening):
    unit_rows = normalize(embeddings)
    chosen_rows = (block_owner.astype(jnp.int32)[:, None] * BLK + landmark_picks.astype(jnp.int32)).reshape(-1)
    landmarks = normalize(jnp.take(candidates, chosen_rows, axis=0))

    def one_block(row_block):
        cosine = jnp.einsum('rd,md->rm', row_block, landmarks, preferred_element_type=jnp.float32)
        kernel = kernel_of(cosine, inverse_width, mixture).astype(jnp.bfloat16)
        return jnp.dot(kernel, whitening, preferred_element_type=jnp.float32).astype(jnp.bfloat16)
    grouped = unit_rows.reshape(ROWS // R_DEV, R_DEV, D)
    result = lax.map(one_block, grouped)
    return result.reshape(ROWS, M)
```

```python
import jax
import jax.numpy as jnp
from jax import lax
from jax.sharding import PartitionSpec as P


def normalize(matrix_rows):
    widened = matrix_rows.astype(jnp.float32)
    scale = lax.rsqrt(jnp.sum(widened * widened, axis=-1, keepdims=True) + 1e-06)
    return (widened * scale).astype(jnp.bfloat16)


def kernel_of(cosine, widths, weights):
    running = jnp.zeros(cosine.shape, jnp.float32)
    for which in range(widths.shape[0]):
        running = running + weights[which] * jnp.exp(2.0 * widths[which] * cosine)
    return running


def inner_products(unit_rows, landmark):
    return jnp.einsum("rd,md->rm", unit_rows, landmark, preferred_element_type=jnp.float32)


def per_device(
    embeddings, candidates, block_owner, landmark_picks, inverse_width, mixture, whitening
):
    unit_rows = normalize(embeddings)
    block_count, block_rows = landmark_picks.shape
    cores = lax.axis_size("bw")
    half = block_rows // cores
    core = lax.axis_index("bw")
    here = lax.axis_index(("row", "lmk"))
    widths = lax.all_gather(inverse_width, "bw", tiled=True)
    weights = lax.all_gather(mixture, "bw", tiled=True)
    pieces = []
    for number in range(block_count):
        picks = lax.dynamic_slice_in_dim(landmark_picks[number], core * half, half)
        chosen = normalize(jnp.take(candidates, picks, axis=0))
        chosen = jnp.where(here == block_owner[number], chosen, jnp.zeros_like(chosen))
        pieces.append(chosen)
    arrived = lax.psum(pieces, ("row", "lmk"))
    blocks = [lax.all_gather(piece, "bw", tiled=True) for piece in arrived]
    kernel = jnp.concatenate(
        [
            kernel_of(inner_products(unit_rows, landmark), widths, weights).astype(jnp.bfloat16)
            for landmark in blocks
        ],
        axis=1,
    )
    features = jnp.dot(kernel, whitening, preferred_element_type=jnp.float32)
    return features.astype(jnp.bfloat16)


def solution(mesh):
    in_specs = (
        P(("row", "lmk"), None),
        P(("row", "lmk"), None),
        P(),
        P(),
        P("bw"),
        P("bw"),
        P(None, "bw"),
    )
    out_specs = P(("row", "lmk"), "bw")
    return jax.shard_map(
        per_device, mesh=mesh, in_specs=in_specs, out_specs=out_specs, check_vma=False
    )
```

```python
import jax
import jax.numpy as jnp
from jax import lax
from jax.sharding import PartitionSpec as P

SPREAD = ("row", "lmk")


def normalize(matrix_rows):
    widened = matrix_rows.astype(jnp.float32)
    scale = lax.rsqrt(jnp.sum(widened * widened, axis=-1, keepdims=True) + 1e-06)
    return (widened * scale).astype(jnp.bfloat16)


def kernel_of(cosine, widths, weights):
    running = jnp.zeros(cosine.shape, jnp.float32)
    for which in range(widths.shape[0]):
        running = running + weights[which] * jnp.exp(2.0 * widths[which] * cosine)
    return running


def inner_products(unit_rows, landmark):
    return jnp.einsum("rd,md->rm", unit_rows, landmark, preferred_element_type=jnp.float32)


def shifted(value, shift, count):
    return lax.ppermute(value, SPREAD, [(i, (i + shift) % count) for i in range(count)])


def broadcast(rows, owner, count):
    here = lax.axis_index(SPREAD)
    pieces = rows.reshape(count, rows.shape[0] // count, rows.shape[1])
    got = [pieces[0] * 0 + lax.dynamic_index_in_dim(pieces, here, 0, keepdims=False)]
    for shift in range(1, count):
        piece = lax.dynamic_index_in_dim(pieces, (here + shift) % count, 0, keepdims=False)
        got.append(shifted(piece, shift, count))
    mine = lax.dynamic_index_in_dim(jnp.stack(got), (here - owner) % count, 0, keepdims=False)
    held = [mine] + [shifted(mine, shift, count) for shift in range(1, count)]
    reordered = jnp.stack([held[0]] + held[:0:-1])
    doubled = jnp.concatenate([reordered, reordered], axis=0)
    whole = lax.dynamic_slice_in_dim(doubled, (count - here) % (2 * count), count, axis=0)
    return whole.reshape(rows.shape)


def per_device(
    embeddings, candidates, block_owner, landmark_picks, inverse_width, mixture, whitening
):
    unit_rows = normalize(embeddings)
    block_count, block_rows = landmark_picks.shape
    cores = lax.axis_size("bw")
    count = lax.axis_size(SPREAD)
    half = block_rows // cores
    core = lax.axis_index("bw")
    widths = lax.all_gather(inverse_width, "bw", tiled=True)
    weights = lax.all_gather(mixture, "bw", tiled=True)
    kernels = []
    for number in range(block_count):
        picks = lax.dynamic_slice_in_dim(landmark_picks[number], core * half, half)
        chosen = normalize(jnp.take(candidates, picks, axis=0))
        mine = broadcast(chosen, block_owner[number], count)
        other = lax.ppermute(mine, "bw", [(0, 1), (1, 0)])
        landmark = jnp.where(
            core == 0,
            jnp.concatenate([mine, other], axis=0),
            jnp.concatenate([other, mine], axis=0),
        )
        kernels.append(
            kernel_of(inner_products(unit_rows, landmark), widths, weights).astype(jnp.bfloat16)
        )
    kernel = jnp.concatenate(kernels, axis=1)
    features = jnp.dot(kernel, whitening, preferred_element_type=jnp.float32)
    return features.astype(jnp.bfloat16)


def solution(mesh):
    in_specs = (
        P(SPREAD, None),
        P(SPREAD, None),
        P(),
        P(),
        P("bw"),
        P("bw"),
        P(None, "bw"),
    )
    out_specs = P(SPREAD, "bw")
    return jax.shard_map(
        per_device, mesh=mesh, in_specs=in_specs, out_specs=out_specs, check_vma=False
    )
```

```python
import jax
import jax.numpy as jnp
from jax import lax
from jax.sharding import PartitionSpec as P

SPREAD = ("row", "lmk")


def normalize(matrix_rows):
    widened = matrix_rows.astype(jnp.float32)
    scale = lax.rsqrt(jnp.sum(widened * widened, axis=-1, keepdims=True) + 1e-06)
    return (widened * scale).astype(jnp.bfloat16)


def kernel_of(cosine, widths, weights):
    running = jnp.zeros(cosine.shape, jnp.float32)
    for which in range(widths.shape[0]):
        running = running + weights[which] * jnp.exp(2.0 * widths[which] * cosine)
    return running


def inner_products(unit_rows, landmark):
    return jnp.einsum("rd,md->rm", unit_rows, landmark, preferred_element_type=jnp.float32)


def select_rows(rows, picks):
    onehot = (picks[:, None] == lax.broadcasted_iota(jnp.int32, (picks.shape[0], rows.shape[0]), 1))
    chosen = jnp.dot(onehot.astype(rows.dtype), rows, preferred_element_type=jnp.float32)
    return chosen.astype(rows.dtype)


def swap_cores(value):
    return lax.ppermute(value, "bw", [(0, 1), (1, 0)])


def per_device(
    embeddings, candidates, block_owner, landmark_picks, inverse_width, mixture, whitening
):
    unit_rows = normalize(embeddings)
    block_count, block_rows = landmark_picks.shape
    cores = lax.axis_size("bw")
    half = block_rows // cores
    core = lax.axis_index("bw")
    here = lax.axis_index(SPREAD)
    widths = jnp.concatenate([inverse_width, swap_cores(inverse_width)])
    weights = jnp.concatenate([mixture, swap_cores(mixture)])
    pieces = []
    for number in range(block_count):
        picks = lax.dynamic_slice_in_dim(landmark_picks[number], core * half, half)
        chosen = normalize(select_rows(candidates, picks))
        chosen = jnp.where(here == block_owner[number], chosen, jnp.zeros_like(chosen))
        pieces.append(chosen)
    arrived = lax.psum(pieces, SPREAD)
    features = jnp.zeros((unit_rows.shape[0], whitening.shape[1]), jnp.float32)
    quarters = []
    for number, mine in enumerate(arrived):
        quarters.append((number, core, mine))
    for number, mine in enumerate(arrived):
        quarters.append((number, 1 - core, swap_cores(mine)))
    for number, which, landmark in quarters:
        kernel = kernel_of(inner_products(unit_rows, landmark), widths, weights).astype(jnp.bfloat16)
        start = number * block_rows + which * half
        rows = lax.dynamic_slice_in_dim(whitening, start, half, axis=0)
        features = features + jnp.dot(kernel, rows, preferred_element_type=jnp.float32)
    return features.astype(jnp.bfloat16)


def solution(mesh):
    in_specs = (
        P(SPREAD, None),
        P(SPREAD, None),
        P(),
        P(),
        P("bw"),
        P("bw"),
        P(None, "bw"),
    )
    out_specs = P(SPREAD, "bw")
    return jax.shard_map(
        per_device, mesh=mesh, in_specs=in_specs, out_specs=out_specs, check_vma=False
    )
```

```python
import jax
import jax.numpy as jnp
from jax import lax
from jax.sharding import PartitionSpec as P

SPREAD = ("row", "lmk")


def normalize(matrix_rows):
    widened = matrix_rows.astype(jnp.float32)
    scale = lax.rsqrt(jnp.sum(widened * widened, axis=-1, keepdims=True) + 1e-06)
    return (widened * scale).astype(jnp.bfloat16)


def kernel_of(cosine, widths, weights):
    scales = 2.0 * widths
    offsets = jnp.log(weights)
    running = jnp.zeros(cosine.shape, jnp.float32)
    for which in range(widths.shape[0]):
        running = running + jnp.exp(scales[which] * cosine + offsets[which])
    return running


def inner_products(unit_rows, landmark):
    return jnp.einsum("rd,md->rm", unit_rows, landmark, preferred_element_type=jnp.float32)


def reorder_columns(kernel, picks, first):
    natural = first + lax.broadcasted_iota(jnp.int32, (kernel.shape[1], picks.shape[0]), 0)
    onehot = (picks[None, :] == natural).astype(kernel.dtype)
    return jnp.dot(kernel, onehot, preferred_element_type=jnp.float32)


def swap_cores(value):
    return lax.ppermute(value, "bw", [(0, 1), (1, 0)])


def per_device(
    embeddings, candidates, block_owner, landmark_picks, inverse_width, mixture, whitening
):
    unit_rows = normalize(embeddings)
    block_count, block_rows = landmark_picks.shape
    cores = lax.axis_size("bw")
    half = block_rows // cores
    core = lax.axis_index("bw")
    here = lax.axis_index(SPREAD)
    widths = jnp.concatenate([inverse_width, swap_cores(inverse_width)])
    weights = jnp.concatenate([mixture, swap_cores(mixture)])
    pieces = []
    for number in range(block_count):
        rows = lax.dynamic_slice_in_dim(candidates, core * half, half, axis=0)
        chosen = normalize(rows)
        chosen = jnp.where(here == block_owner[number], chosen, jnp.zeros_like(chosen))
        pieces.append(chosen)
    arrived = lax.psum(pieces, SPREAD)
    features = jnp.zeros((unit_rows.shape[0], whitening.shape[1]), jnp.float32)
    for number, mine in enumerate(arrived):
        ordered = jnp.zeros((unit_rows.shape[0], block_rows), jnp.float32)
        for which, landmark in ((core, mine), (1 - core, swap_cores(mine))):
            kernel = kernel_of(inner_products(unit_rows, landmark), widths, weights)
            ordered = ordered + reorder_columns(
                kernel.astype(jnp.bfloat16), landmark_picks[number], which * half
            )
        rows = lax.dynamic_slice_in_dim(whitening, number * block_rows, block_rows, axis=0)
        features = features + jnp.dot(
            ordered.astype(jnp.bfloat16), rows, preferred_element_type=jnp.float32
        )
    return features.astype(jnp.bfloat16)


def solution(mesh):
    in_specs = (
        P(SPREAD, None),
        P(SPREAD, None),
        P(),
        P(),
        P("bw"),
        P("bw"),
        P(None, "bw"),
    )
    out_specs = P(SPREAD, "bw")
    return jax.shard_map(
        per_device, mesh=mesh, in_specs=in_specs, out_specs=out_specs, check_vma=False
    )
```

```python
import jax
import jax.numpy as jnp
from jax import lax
from jax.sharding import PartitionSpec as P

SPREAD = ("row", "lmk")


def normalize(matrix_rows):
    widened = matrix_rows.astype(jnp.float32)
    scale = lax.rsqrt(jnp.sum(widened * widened, axis=-1, keepdims=True) + 1e-06)
    return (widened * scale).astype(jnp.bfloat16)


def kernel_of(cosine, widths, weights):
    scales = 2.0 * widths
    offsets = jnp.log(weights)
    running = jnp.zeros(cosine.shape, jnp.float32)
    for which in range(widths.shape[0]):
        running = running + jnp.exp(scales[which] * cosine + offsets[which])
    return running


def inner_products(unit_rows, landmark):
    return jnp.einsum("rd,md->rm", unit_rows, landmark, preferred_element_type=jnp.float32)


def reorder_columns(kernel, picks, first):
    natural = first + lax.broadcasted_iota(jnp.int32, (kernel.shape[1], picks.shape[0]), 0)
    onehot = (picks[None, :] == natural).astype(kernel.dtype)
    return jnp.dot(kernel, onehot, preferred_element_type=jnp.float32)


def swap_cores(value):
    return lax.ppermute(value, "bw", [(0, 1), (1, 0)])


def per_device(
    embeddings, candidates, block_owner, landmark_picks, inverse_width, mixture, whitening
):
    unit_rows = normalize(embeddings)
    block_count, block_rows = landmark_picks.shape
    cores = lax.axis_size("bw")
    half = block_rows // cores
    core = lax.axis_index("bw")
    here = lax.axis_index(SPREAD)
    widths = jnp.concatenate([inverse_width, swap_cores(inverse_width)])
    weights = jnp.concatenate([mixture, swap_cores(mixture)])
    pieces = []
    for number in range(block_count):
        rows = lax.dynamic_slice_in_dim(candidates, core * half, half, axis=0)
        chosen = normalize(rows)
        chosen = jnp.where(here == block_owner[number], chosen, jnp.zeros_like(chosen))
        pieces.append(chosen)
    arrived = lax.psum(pieces, SPREAD)
    features = jnp.zeros((unit_rows.shape[0], whitening.shape[1]), jnp.float32)
    for number, mine in enumerate(arrived):
        ordered = jnp.zeros((unit_rows.shape[0], block_rows), jnp.float32)
        for which, landmark in ((core, mine), (1 - core, swap_cores(mine))):
            kernel = kernel_of(inner_products(unit_rows, landmark), widths, weights)
            kernel = lax.optimization_barrier(kernel.astype(jnp.bfloat16))
            ordered = ordered + reorder_columns(kernel, landmark_picks[number], which * half)
        rows = lax.dynamic_slice_in_dim(whitening, number * block_rows, block_rows, axis=0)
        features = features + jnp.dot(
            ordered.astype(jnp.bfloat16), rows, preferred_element_type=jnp.float32
        )
    return features.astype(jnp.bfloat16)


def solution(mesh):
    in_specs = (
        P(SPREAD, None),
        P(SPREAD, None),
        P(),
        P(),
        P("bw"),
        P("bw"),
        P(None, "bw"),
    )
    out_specs = P(SPREAD, "bw")
    return jax.shard_map(
        per_device, mesh=mesh, in_specs=in_specs, out_specs=out_specs, check_vma=False
    )
```

```python
import jax
import jax.numpy as jnp
from jax import lax
from jax.sharding import PartitionSpec as P

SPREAD = ("row", "lmk")


def normalize(matrix_rows):
    widened = matrix_rows.astype(jnp.float32)
    scale = lax.rsqrt(jnp.sum(widened * widened, axis=-1, keepdims=True) + 1e-06)
    return (widened * scale).astype(jnp.bfloat16)


def kernel_of(cosine, widths, weights):
    running = jnp.zeros(cosine.shape, jnp.float32)
    for which in range(widths.shape[0]):
        running = running + weights[which] * jnp.exp(2.0 * widths[which] * cosine)
    return running


def inner_products(unit_rows, landmark):
    return jnp.einsum("rd,md->rm", unit_rows, landmark, preferred_element_type=jnp.float32)


def select_rows(rows, picks):
    onehot = (picks[:, None] == lax.broadcasted_iota(jnp.int32, (picks.shape[0], rows.shape[0]), 1))
    chosen = jnp.dot(onehot.astype(rows.dtype), rows, preferred_element_type=jnp.float32)
    return chosen.astype(rows.dtype)


def swap_cores(value):
    return lax.ppermute(value, "bw", [(0, 1), (1, 0)])


def per_device(
    embeddings, candidates, block_owner, landmark_picks, inverse_width, mixture, whitening
):
    unit_rows = normalize(embeddings)
    block_count, block_rows = landmark_picks.shape
    cores = lax.axis_size("bw")
    half = block_rows // cores
    core = lax.axis_index("bw")
    here = lax.axis_index(SPREAD)
    widths = jnp.concatenate([inverse_width, swap_cores(inverse_width)])
    weights = jnp.concatenate([mixture, swap_cores(mixture)])
    pieces = []
    for number in range(block_count):
        picks = lax.dynamic_slice_in_dim(landmark_picks[number], core * half, half)
        chosen = normalize(select_rows(candidates, picks))
        chosen = jnp.where(here == block_owner[number], chosen, jnp.zeros_like(chosen))
        pieces.append(chosen)
    arrived = lax.psum(pieces, SPREAD)
    share = unit_rows.shape[0] // cores
    own_rows = lax.dynamic_slice_in_dim(unit_rows, core * share, share, axis=0)
    features = jnp.zeros((unit_rows.shape[0], whitening.shape[1]), jnp.float32)
    for number, mine in enumerate(arrived):
        other = swap_cores(mine)
        parts = [
            kernel_of(inner_products(own_rows, landmark), widths, weights).astype(jnp.bfloat16)
            for landmark in (mine, other)
        ]
        own_kernel = jnp.where(
            core == 0,
            jnp.concatenate(parts, axis=1),
            jnp.concatenate(parts[::-1], axis=1),
        )
        other_kernel = swap_cores(own_kernel)
        kernel = jnp.where(
            core == 0,
            jnp.concatenate([own_kernel, other_kernel], axis=0),
            jnp.concatenate([other_kernel, own_kernel], axis=0),
        )
        rows = lax.dynamic_slice_in_dim(whitening, number * block_rows, block_rows, axis=0)
        features = features + jnp.dot(kernel, rows, preferred_element_type=jnp.float32)
    return features.astype(jnp.bfloat16)


def solution(mesh):
    in_specs = (
        P(SPREAD, None),
        P(SPREAD, None),
        P(),
        P(),
        P("bw"),
        P("bw"),
        P(None, "bw"),
    )
    out_specs = P(SPREAD, "bw")
    return jax.shard_map(
        per_device, mesh=mesh, in_specs=in_specs, out_specs=out_specs, check_vma=False
    )
```

```python
import jax
import jax.numpy as jnp
from jax import lax
from jax.sharding import PartitionSpec as P

SPREAD = ("row", "lmk")


def normalize(matrix_rows):
    widened = matrix_rows.astype(jnp.float32)
    scale = lax.rsqrt(jnp.sum(widened * widened, axis=-1, keepdims=True) + 1e-06)
    return (widened * scale).astype(jnp.bfloat16)


def kernel_of(cosine, widths, weights):
    running = jnp.zeros(cosine.shape, jnp.float32)
    for which in range(widths.shape[0]):
        running = running + weights[which] * jnp.exp(2.0 * widths[which] * cosine)
    return running


def inner_products(unit_rows, landmark):
    return jnp.einsum("rd,md->rm", unit_rows, landmark, preferred_element_type=jnp.float32)


def reorder_columns(kernel, picks):
    natural = lax.broadcasted_iota(jnp.int32, (kernel.shape[1], picks.shape[0]), 0)
    onehot = (picks[None, :] == natural).astype(kernel.dtype)
    ordered = jnp.dot(kernel, onehot, preferred_element_type=jnp.float32)
    return ordered.astype(kernel.dtype)


def swap_cores(value):
    return lax.ppermute(value, "bw", [(0, 1), (1, 0)])


def per_device(
    embeddings, candidates, block_owner, landmark_picks, inverse_width, mixture, whitening
):
    unit_rows = normalize(embeddings)
    block_count, block_rows = landmark_picks.shape
    cores = lax.axis_size("bw")
    half = block_rows // cores
    core = lax.axis_index("bw")
    here = lax.axis_index(SPREAD)
    widths = jnp.concatenate([inverse_width, swap_cores(inverse_width)])
    weights = jnp.concatenate([mixture, swap_cores(mixture)])
    pieces = []
    for number in range(block_count):
        chosen = normalize(lax.dynamic_slice_in_dim(candidates, core * half, half, axis=0))
        chosen = jnp.where(here == block_owner[number], chosen, jnp.zeros_like(chosen))
        pieces.append(chosen)
    arrived = lax.psum(pieces, SPREAD)
    share = unit_rows.shape[0] // cores
    own_rows = lax.dynamic_slice_in_dim(unit_rows, core * share, share, axis=0)
    features = jnp.zeros((unit_rows.shape[0], whitening.shape[1]), jnp.float32)
    for number, mine in enumerate(arrived):
        other = swap_cores(mine)
        parts = [
            kernel_of(inner_products(own_rows, landmark), widths, weights).astype(jnp.bfloat16)
            for landmark in (mine, other)
        ]
        own_kernel = jnp.where(
            core == 0,
            jnp.concatenate(parts, axis=1),
            jnp.concatenate(parts[::-1], axis=1),
        )
        own_kernel = reorder_columns(own_kernel, landmark_picks[number])
        other_kernel = swap_cores(own_kernel)
        kernel = jnp.where(
            core == 0,
            jnp.concatenate([own_kernel, other_kernel], axis=0),
            jnp.concatenate([other_kernel, own_kernel], axis=0),
        )
        rows = lax.dynamic_slice_in_dim(whitening, number * block_rows, block_rows, axis=0)
        features = features + jnp.dot(kernel, rows, preferred_element_type=jnp.float32)
    return features.astype(jnp.bfloat16)


def solution(mesh):
    in_specs = (
        P(SPREAD, None),
        P(SPREAD, None),
        P(),
        P(),
        P("bw"),
        P("bw"),
        P(None, "bw"),
    )
    out_specs = P(SPREAD, "bw")
    return jax.shard_map(
        per_device, mesh=mesh, in_specs=in_specs, out_specs=out_specs, check_vma=False
    )
```

```python
import jax
import jax.numpy as jnp
from jax import lax
from jax.sharding import PartitionSpec as P

SPREAD = ("row", "lmk")


def normalize(matrix_rows):
    widened = matrix_rows.astype(jnp.float32)
    scale = lax.rsqrt(jnp.sum(widened * widened, axis=-1, keepdims=True) + 1e-06)
    return (widened * scale).astype(jnp.bfloat16)


def kernel_of(cosine, widths, weights):
    running = jnp.zeros(cosine.shape, jnp.float32)
    for which in range(widths.shape[0]):
        running = running + weights[which] * jnp.exp(2.0 * widths[which] * cosine)
    return running


def inner_products(unit_rows, landmark):
    return jnp.einsum("rd,md->rm", unit_rows, landmark, preferred_element_type=jnp.float32)


def reorder_columns(kernel, picks):
    natural = lax.broadcasted_iota(jnp.int32, (kernel.shape[1], picks.shape[0]), 0)
    onehot = (picks[None, :] == natural).astype(kernel.dtype)
    ordered = jnp.dot(kernel, onehot, preferred_element_type=jnp.float32)
    return ordered.astype(kernel.dtype)


def swap_cores(value):
    return lax.ppermute(value, "bw", [(0, 1), (1, 0)])


def per_device(
    embeddings, candidates, block_owner, landmark_picks, inverse_width, mixture, whitening
):
    unit_rows = normalize(embeddings)
    block_count, block_rows = landmark_picks.shape
    cores = lax.axis_size("bw")
    half = block_rows // cores
    core = lax.axis_index("bw")
    here = lax.axis_index(SPREAD)
    widths = jnp.concatenate([inverse_width, swap_cores(inverse_width)])
    weights = jnp.concatenate([mixture, swap_cores(mixture)])
    pieces = []
    for number in range(block_count):
        chosen = normalize(lax.dynamic_slice_in_dim(candidates, core * half, half, axis=0))
        chosen = jnp.where(here == block_owner[number], chosen, jnp.zeros_like(chosen))
        pieces.append(chosen)
    pieces, widths, weights = lax.optimization_barrier((pieces, widths, weights))
    arrived = lax.psum(pieces, SPREAD)
    share = unit_rows.shape[0] // cores
    own_rows = lax.dynamic_slice_in_dim(unit_rows, core * share, share, axis=0)
    features = jnp.zeros((unit_rows.shape[0], whitening.shape[1]), jnp.float32)
    for number, mine in enumerate(arrived):
        other = swap_cores(mine)
        parts = [
            kernel_of(inner_products(own_rows, landmark), widths, weights).astype(jnp.bfloat16)
            for landmark in (mine, other)
        ]
        own_kernel = jnp.where(
            core == 0,
            jnp.concatenate(parts, axis=1),
            jnp.concatenate(parts[::-1], axis=1),
        )
        own_kernel = reorder_columns(own_kernel, landmark_picks[number])
        other_kernel = swap_cores(own_kernel)
        kernel = jnp.where(
            core == 0,
            jnp.concatenate([own_kernel, other_kernel], axis=0),
            jnp.concatenate([other_kernel, own_kernel], axis=0),
        )
        rows = lax.dynamic_slice_in_dim(whitening, number * block_rows, block_rows, axis=0)
        features = features + jnp.dot(kernel, rows, preferred_element_type=jnp.float32)
    return features.astype(jnp.bfloat16)


def solution(mesh):
    in_specs = (
        P(SPREAD, None),
        P(SPREAD, None),
        P(),
        P(),
        P("bw"),
        P("bw"),
        P(None, "bw"),
    )
    out_specs = P(SPREAD, "bw")
    return jax.shard_map(
        per_device, mesh=mesh, in_specs=in_specs, out_specs=out_specs, check_vma=False
    )
```

```python
import jax
import jax.numpy as jnp
from jax import lax
from jax.sharding import PartitionSpec as P

SPREAD = ("row", "lmk")


def normalize(matrix_rows):
    widened = matrix_rows.astype(jnp.float32)
    scale = lax.rsqrt(jnp.sum(widened * widened, axis=-1, keepdims=True) + 1e-06)
    return (widened * scale).astype(jnp.bfloat16)


def kernel_of(cosine, widths, weights):
    running = jnp.zeros(cosine.shape, jnp.float32)
    for which in range(widths.shape[0]):
        running = running + weights[which] * jnp.exp(2.0 * widths[which] * cosine)
    return running


def inner_products(unit_rows, landmark):
    return jnp.einsum("rd,md->rm", unit_rows, landmark, preferred_element_type=jnp.float32)


def reorder_columns(kernel, picks):
    natural = lax.broadcasted_iota(jnp.int32, (kernel.shape[1], picks.shape[0]), 0)
    onehot = (picks[None, :] == natural).astype(kernel.dtype)
    ordered = jnp.dot(kernel, onehot, preferred_element_type=jnp.float32)
    return ordered.astype(kernel.dtype)


def swap_cores(value):
    return lax.ppermute(value, "bw", [(0, 1), (1, 0)])


def per_device(
    embeddings, candidates, block_owner, landmark_picks, inverse_width, mixture, whitening
):
    unit_rows = normalize(embeddings)
    block_count, block_rows = landmark_picks.shape
    cores = lax.axis_size("bw")
    half = block_rows // cores
    core = lax.axis_index("bw")
    here = lax.axis_index(SPREAD)
    widths = jnp.concatenate([inverse_width, swap_cores(inverse_width)])
    weights = jnp.concatenate([mixture, swap_cores(mixture)])
    pieces = []
    for number in range(block_count):
        chosen = normalize(lax.dynamic_slice_in_dim(candidates, core * half, half, axis=0))
        chosen = jnp.where(here == block_owner[number], chosen, jnp.zeros_like(chosen))
        pieces.append(chosen)
    pieces, widths, weights = lax.optimization_barrier((pieces, widths, weights))
    orders = [SPREAD, SPREAD[::-1]]
    arrived = [lax.psum(piece, orders[number % 2]) for number, piece in enumerate(pieces)]
    share = unit_rows.shape[0] // cores
    own_rows = lax.dynamic_slice_in_dim(unit_rows, core * share, share, axis=0)
    features = jnp.zeros((unit_rows.shape[0], whitening.shape[1]), jnp.float32)
    for number, mine in enumerate(arrived):
        other = swap_cores(mine)
        parts = [
            kernel_of(inner_products(own_rows, landmark), widths, weights).astype(jnp.bfloat16)
            for landmark in (mine, other)
        ]
        own_kernel = jnp.where(
            core == 0,
            jnp.concatenate(parts, axis=1),
            jnp.concatenate(parts[::-1], axis=1),
        )
        own_kernel = reorder_columns(own_kernel, landmark_picks[number])
        other_kernel = swap_cores(own_kernel)
        kernel = jnp.where(
            core == 0,
            jnp.concatenate([own_kernel, other_kernel], axis=0),
            jnp.concatenate([other_kernel, own_kernel], axis=0),
        )
        rows = lax.dynamic_slice_in_dim(whitening, number * block_rows, block_rows, axis=0)
        features = features + jnp.dot(kernel, rows, preferred_element_type=jnp.float32)
    return features.astype(jnp.bfloat16)


def solution(mesh):
    in_specs = (
        P(SPREAD, None),
        P(SPREAD, None),
        P(),
        P(),
        P("bw"),
        P("bw"),
        P(None, "bw"),
    )
    out_specs = P(SPREAD, "bw")
    return jax.shard_map(
        per_device, mesh=mesh, in_specs=in_specs, out_specs=out_specs, check_vma=False
    )
```

```python
import jax
import jax.numpy as jnp
from jax import lax
from jax.sharding import PartitionSpec as P

SPREAD = ("row", "lmk")


def normalize(matrix_rows):
    widened = matrix_rows.astype(jnp.float32)
    scale = lax.rsqrt(jnp.sum(widened * widened, axis=-1, keepdims=True) + 1e-06)
    return (widened * scale).astype(jnp.bfloat16)


def kernel_of(cosine, widths, weights):
    running = jnp.zeros(cosine.shape, jnp.float32)
    for which in range(widths.shape[0]):
        running = running + weights[which] * jnp.exp(2.0 * widths[which] * cosine)
    return running


def inner_products(unit_rows, landmark):
    return jnp.einsum("rd,md->rm", unit_rows, landmark, preferred_element_type=jnp.float32)


def reorder_columns(kernel, picks):
    natural = lax.broadcasted_iota(jnp.int32, (kernel.shape[1], picks.shape[0]), 0)
    onehot = (picks[None, :] == natural).astype(kernel.dtype)
    ordered = jnp.dot(kernel, onehot, preferred_element_type=jnp.float32)
    return ordered.astype(kernel.dtype)


def swap_cores(value):
    return lax.ppermute(value, "bw", [(0, 1), (1, 0)])


def per_device(
    embeddings, candidates, block_owner, landmark_picks, inverse_width, mixture, whitening
):
    unit_rows = normalize(embeddings)
    block_count, block_rows = landmark_picks.shape
    cores = lax.axis_size("bw")
    half = block_rows // cores
    core = lax.axis_index("bw")
    here = lax.axis_index(SPREAD)
    widths = jnp.concatenate([inverse_width, swap_cores(inverse_width)])
    weights = jnp.concatenate([mixture, swap_cores(mixture)])
    count = lax.axis_size(SPREAD)
    chosen = normalize(lax.dynamic_slice_in_dim(candidates, core * half, half, axis=0))
    chosen, widths, weights = lax.optimization_barrier((chosen, widths, weights))
    pieces = chosen.reshape(count, half // count, chosen.shape[1])
    spread = lax.all_to_all(pieces, SPREAD, 0, 0, tiled=True)
    kept = jnp.stack(
        [
            lax.dynamic_index_in_dim(spread, block_owner[number], 0, keepdims=False)
            for number in range(block_count)
        ]
    )
    gathered = lax.all_to_all(
        jnp.broadcast_to(kept[None], (count,) + kept.shape), SPREAD, 0, 0, tiled=True
    )
    arrived = [gathered[:, number].reshape(half, chosen.shape[1]) for number in range(block_count)]
    share = unit_rows.shape[0] // cores
    own_rows = lax.dynamic_slice_in_dim(unit_rows, core * share, share, axis=0)
    features = jnp.zeros((unit_rows.shape[0], whitening.shape[1]), jnp.float32)
    for number, mine in enumerate(arrived):
        other = swap_cores(mine)
        parts = [
            kernel_of(inner_products(own_rows, landmark), widths, weights).astype(jnp.bfloat16)
            for landmark in (mine, other)
        ]
        own_kernel = jnp.where(
            core == 0,
            jnp.concatenate(parts, axis=1),
            jnp.concatenate(parts[::-1], axis=1),
        )
        own_kernel = reorder_columns(own_kernel, landmark_picks[number])
        other_kernel = swap_cores(own_kernel)
        kernel = jnp.where(
            core == 0,
            jnp.concatenate([own_kernel, other_kernel], axis=0),
            jnp.concatenate([other_kernel, own_kernel], axis=0),
        )
        rows = lax.dynamic_slice_in_dim(whitening, number * block_rows, block_rows, axis=0)
        features = features + jnp.dot(kernel, rows, preferred_element_type=jnp.float32)
    return features.astype(jnp.bfloat16)


def solution(mesh):
    in_specs = (
        P(SPREAD, None),
        P(SPREAD, None),
        P(),
        P(),
        P("bw"),
        P("bw"),
        P(None, "bw"),
    )
    out_specs = P(SPREAD, "bw")
    return jax.shard_map(
        per_device, mesh=mesh, in_specs=in_specs, out_specs=out_specs, check_vma=False
    )
```

```python
import jax
import jax.numpy as jnp
from jax import lax
from jax.sharding import PartitionSpec as P

SPREAD = ("row", "lmk")


def normalize(matrix_rows):
    widened = matrix_rows.astype(jnp.float32)
    scale = lax.rsqrt(jnp.sum(widened * widened, axis=-1, keepdims=True) + 1e-06)
    return (widened * scale).astype(jnp.bfloat16)


def kernel_of(cosine, widths, weights):
    running = jnp.zeros(cosine.shape, jnp.float32)
    for which in range(widths.shape[0]):
        running = running + weights[which] * jnp.exp(2.0 * widths[which] * cosine)
    return running


def inner_products(unit_rows, landmark):
    return jnp.einsum("rd,md->rm", unit_rows, landmark, preferred_element_type=jnp.float32)


def reorder_columns(kernel, picks):
    natural = lax.broadcasted_iota(jnp.int32, (kernel.shape[1], picks.shape[0]), 0)
    onehot = (picks[None, :] == natural).astype(kernel.dtype)
    ordered = jnp.dot(kernel, onehot, preferred_element_type=jnp.float32)
    return ordered.astype(kernel.dtype)


def swap_cores(value):
    return lax.ppermute(value, "bw", [(0, 1), (1, 0)])


def per_device(
    embeddings, candidates, block_owner, landmark_picks, inverse_width, mixture, whitening
):
    unit_rows = normalize(embeddings)
    block_count, block_rows = landmark_picks.shape
    cores = lax.axis_size("bw")
    half = block_rows // cores
    core = lax.axis_index("bw")
    here = lax.axis_index(SPREAD)
    widths = jnp.concatenate([inverse_width, swap_cores(inverse_width)])
    weights = jnp.concatenate([mixture, swap_cores(mixture)])
    count = lax.axis_size(SPREAD)
    chosen = lax.dynamic_slice_in_dim(candidates, core * half, half, axis=0)
    pieces = chosen.reshape(count, half // count, chosen.shape[1])
    spread = lax.all_to_all(pieces, SPREAD, 0, 0, tiled=True)
    kept = jnp.stack(
        [
            normalize(lax.dynamic_index_in_dim(spread, block_owner[number], 0, keepdims=False))
            for number in range(block_count)
        ]
    )
    kept, widths, weights = lax.optimization_barrier((kept, widths, weights))
    gathered = lax.all_to_all(
        jnp.broadcast_to(kept[None], (count,) + kept.shape), SPREAD, 0, 0, tiled=True
    )
    arrived = [gathered[:, number].reshape(half, chosen.shape[1]) for number in range(block_count)]
    share = unit_rows.shape[0] // cores
    own_rows = lax.dynamic_slice_in_dim(unit_rows, core * share, share, axis=0)
    features = jnp.zeros((unit_rows.shape[0], whitening.shape[1]), jnp.float32)
    for number, mine in enumerate(arrived):
        other = swap_cores(mine)
        parts = [
            kernel_of(inner_products(own_rows, landmark), widths, weights).astype(jnp.bfloat16)
            for landmark in (mine, other)
        ]
        own_kernel = jnp.where(
            core == 0,
            jnp.concatenate(parts, axis=1),
            jnp.concatenate(parts[::-1], axis=1),
        )
        own_kernel = reorder_columns(own_kernel, landmark_picks[number])
        other_kernel = swap_cores(own_kernel)
        kernel = jnp.where(
            core == 0,
            jnp.concatenate([own_kernel, other_kernel], axis=0),
            jnp.concatenate([other_kernel, own_kernel], axis=0),
        )
        rows = lax.dynamic_slice_in_dim(whitening, number * block_rows, block_rows, axis=0)
        features = features + jnp.dot(kernel, rows, preferred_element_type=jnp.float32)
    return features.astype(jnp.bfloat16)


def solution(mesh):
    in_specs = (
        P(SPREAD, None),
        P(SPREAD, None),
        P(),
        P(),
        P("bw"),
        P("bw"),
        P(None, "bw"),
    )
    out_specs = P(SPREAD, "bw")
    return jax.shard_map(
        per_device, mesh=mesh, in_specs=in_specs, out_specs=out_specs, check_vma=False
    )
```

```python
import jax
import jax.numpy as jnp
from jax import lax
from jax.sharding import PartitionSpec as P

SPREAD = ("row", "lmk")


def normalize(matrix_rows):
    widened = matrix_rows.astype(jnp.float32)
    scale = lax.rsqrt(jnp.sum(widened * widened, axis=-1, keepdims=True) + 1e-06)
    return (widened * scale).astype(jnp.bfloat16)


def kernel_of(cosine, widths, weights):
    running = jnp.zeros(cosine.shape, jnp.float32)
    for which in range(widths.shape[0]):
        running = running + weights[which] * jnp.exp(2.0 * widths[which] * cosine)
    return running


def inner_products(unit_rows, landmark):
    return jnp.einsum("rd,md->rm", unit_rows, landmark, preferred_element_type=jnp.float32)


def reorder_columns(kernel, picks):
    natural = lax.broadcasted_iota(jnp.int32, (kernel.shape[1], picks.shape[0]), 0)
    onehot = (picks[None, :] == natural).astype(kernel.dtype)
    ordered = jnp.dot(kernel, onehot, preferred_element_type=jnp.float32)
    return ordered.astype(kernel.dtype)


def swap_cores(value):
    return lax.ppermute(value, "bw", [(0, 1), (1, 0)])


def per_device(
    embeddings, candidates, block_owner, landmark_picks, inverse_width, mixture, whitening
):
    unit_rows = normalize(embeddings)
    block_count, block_rows = landmark_picks.shape
    cores = lax.axis_size("bw")
    half = block_rows // cores
    core = lax.axis_index("bw")
    here = lax.axis_index(SPREAD)
    widths = jnp.concatenate([inverse_width, swap_cores(inverse_width)])
    weights = jnp.concatenate([mixture, swap_cores(mixture)])
    count = lax.axis_size(SPREAD)
    chosen = normalize(lax.dynamic_slice_in_dim(candidates, core * half, half, axis=0))
    chosen, widths, weights = lax.optimization_barrier((chosen, widths, weights))
    pieces = chosen.reshape(count, half // count, chosen.shape[1])
    spread = lax.all_to_all(pieces, SPREAD, 0, 0, tiled=True)
    kept = jnp.stack(
        [
            lax.dynamic_index_in_dim(spread, block_owner[number], 0, keepdims=False)
            for number in range(block_count)
        ]
    )
    arrived = [
        lax.all_to_all(
            jnp.broadcast_to(kept[number][None], (count,) + kept.shape[1:]), SPREAD, 0, 0, tiled=True
        ).reshape(half, chosen.shape[1])
        for number in range(block_count)
    ]
    share = unit_rows.shape[0] // cores
    own_rows = lax.dynamic_slice_in_dim(unit_rows, core * share, share, axis=0)
    features = jnp.zeros((unit_rows.shape[0], whitening.shape[1]), jnp.float32)
    for number in range(block_count):
        mine = arrived[number]
        if number > 0:
            mine, features = lax.optimization_barrier((mine, features))
        other = swap_cores(mine)
        parts = [
            kernel_of(inner_products(own_rows, landmark), widths, weights).astype(jnp.bfloat16)
            for landmark in (mine, other)
        ]
        own_kernel = jnp.where(
            core == 0,
            jnp.concatenate(parts, axis=1),
            jnp.concatenate(parts[::-1], axis=1),
        )
        own_kernel = reorder_columns(own_kernel, landmark_picks[number])
        other_kernel = swap_cores(own_kernel)
        kernel = jnp.where(
            core == 0,
            jnp.concatenate([own_kernel, other_kernel], axis=0),
            jnp.concatenate([other_kernel, own_kernel], axis=0),
        )
        rows = lax.dynamic_slice_in_dim(whitening, number * block_rows, block_rows, axis=0)
        features = features + jnp.dot(kernel, rows, preferred_element_type=jnp.float32)
    return features.astype(jnp.bfloat16)


def solution(mesh):
    in_specs = (
        P(SPREAD, None),
        P(SPREAD, None),
        P(),
        P(),
        P("bw"),
        P("bw"),
        P(None, "bw"),
    )
    out_specs = P(SPREAD, "bw")
    return jax.shard_map(
        per_device, mesh=mesh, in_specs=in_specs, out_specs=out_specs, check_vma=False
    )
```

```python
import jax
import jax.numpy as jnp
from jax import lax
from jax.sharding import PartitionSpec as P

SPREAD = ("row", "lmk")


def normalize(matrix_rows):
    widened = matrix_rows.astype(jnp.float32)
    scale = lax.rsqrt(jnp.sum(widened * widened, axis=-1, keepdims=True) + 1e-06)
    return (widened * scale).astype(jnp.bfloat16)


def kernel_of(cosine, widths, weights):
    running = jnp.zeros(cosine.shape, jnp.float32)
    for which in range(widths.shape[0]):
        running = running + weights[which] * jnp.exp(2.0 * widths[which] * cosine)
    return running


def inner_products(unit_rows, landmark):
    return jnp.einsum("rd,md->rm", unit_rows, landmark, preferred_element_type=jnp.float32)


def reorder_columns(kernel, natural, picks):
    onehot = (picks[None, :] == natural[:, None]).astype(kernel.dtype)
    return jnp.dot(kernel, onehot, preferred_element_type=jnp.float32)


def swap_cores(value):
    return lax.ppermute(value, "bw", [(0, 1), (1, 0)])


def per_device(
    embeddings, candidates, block_owner, landmark_picks, inverse_width, mixture, whitening
):
    unit_rows = normalize(embeddings)
    block_count, block_rows = landmark_picks.shape
    cores = lax.axis_size("bw")
    half = block_rows // cores
    core = lax.axis_index("bw")
    here = lax.axis_index(SPREAD)
    widths = jnp.concatenate([inverse_width, swap_cores(inverse_width)])
    weights = jnp.concatenate([mixture, swap_cores(mixture)])
    count = lax.axis_size(SPREAD)
    chosen = normalize(lax.dynamic_slice_in_dim(candidates, core * half, half, axis=0))
    chosen, widths, weights = lax.optimization_barrier((chosen, widths, weights))
    pieces = chosen.reshape(count, half // count, chosen.shape[1])
    spread = lax.all_to_all(pieces, SPREAD, 0, 0, tiled=True)
    kept = jnp.stack(
        [
            lax.dynamic_index_in_dim(spread, block_owner[number], 0, keepdims=False)
            for number in range(block_count)
        ]
    )
    piece_rows = half // count
    splits = 2
    part = piece_rows // splits
    share = unit_rows.shape[0] // cores
    own_rows = lax.dynamic_slice_in_dim(unit_rows, core * share, share, axis=0)

    def natural_rows(which, chunk):
        piece = lax.broadcasted_iota(jnp.int32, (count, part), 0)
        inner = lax.broadcasted_iota(jnp.int32, (count, part), 1)
        return (which * half + piece * piece_rows + chunk * part + inner).reshape(-1)

    units = [(number, chunk) for number in range(block_count) for chunk in range(splits)]
    gathered = [
        lax.all_to_all(
            jnp.broadcast_to(
                kept[number, chunk * part:(chunk + 1) * part][None], (count, part, kept.shape[2])
            ),
            SPREAD, 0, 0, tiled=True,
        ).reshape(count * part, kept.shape[2])
        for number, chunk in units
    ]
    features = jnp.zeros((unit_rows.shape[0], whitening.shape[1]), jnp.float32)
    ordered = jnp.zeros((share, block_rows), jnp.float32)
    for step, (number, chunk) in enumerate(units):
        mine = gathered[step]
        if step > 0:
            mine, features, ordered = lax.optimization_barrier((mine, features, ordered))
        other = swap_cores(mine)
        kernel = kernel_of(
            inner_products(own_rows, jnp.concatenate([mine, other], axis=0)), widths, weights
        ).astype(jnp.bfloat16)
        kernel = lax.optimization_barrier(kernel)
        natural = jnp.concatenate([natural_rows(core, chunk), natural_rows(1 - core, chunk)])
        ordered = ordered + reorder_columns(kernel, natural, landmark_picks[number])
        if chunk == splits - 1:
            own_kernel = ordered.astype(jnp.bfloat16)
            other_kernel = swap_cores(own_kernel)
            kernel = jnp.where(
                core == 0,
                jnp.concatenate([own_kernel, other_kernel], axis=0),
                jnp.concatenate([other_kernel, own_kernel], axis=0),
            )
            rows = lax.dynamic_slice_in_dim(whitening, number * block_rows, block_rows, axis=0)
            features = features + jnp.dot(kernel, rows, preferred_element_type=jnp.float32)
            ordered = jnp.zeros((share, block_rows), jnp.float32)
    return features.astype(jnp.bfloat16)


def solution(mesh):
    in_specs = (
        P(SPREAD, None),
        P(SPREAD, None),
        P(),
        P(),
        P("bw"),
        P("bw"),
        P(None, "bw"),
    )
    out_specs = P(SPREAD, "bw")
    return jax.shard_map(
        per_device, mesh=mesh, in_specs=in_specs, out_specs=out_specs, check_vma=False
    )
```

```python
import jax
import jax.numpy as jnp
from jax import lax
from jax.sharding import PartitionSpec as P

SPREAD = ("row", "lmk")


def normalize(matrix_rows):
    widened = matrix_rows.astype(jnp.float32)
    scale = lax.rsqrt(jnp.sum(widened * widened, axis=-1, keepdims=True) + 1e-06)
    return (widened * scale).astype(jnp.bfloat16)


def kernel_of(cosine, widths, weights):
    running = jnp.zeros(cosine.shape, jnp.float32)
    for which in range(widths.shape[0]):
        running = running + weights[which] * jnp.exp(2.0 * widths[which] * cosine)
    return running


def inner_products(unit_rows, landmark):
    return jnp.einsum("rd,md->rm", unit_rows, landmark, preferred_element_type=jnp.float32)


def reorder_columns(kernel, picks):
    natural = lax.broadcasted_iota(jnp.int32, (kernel.shape[1], picks.shape[0]), 0)
    onehot = (picks[None, :] == natural).astype(kernel.dtype)
    ordered = jnp.dot(kernel, onehot, preferred_element_type=jnp.float32)
    return ordered.astype(kernel.dtype)


def swap_cores(value):
    return lax.ppermute(value, "bw", [(0, 1), (1, 0)])


def per_device(
    embeddings, candidates, block_owner, landmark_picks, inverse_width, mixture, whitening
):
    unit_rows = normalize(embeddings)
    block_count, block_rows = landmark_picks.shape
    cores = lax.axis_size("bw")
    half = block_rows // cores
    core = lax.axis_index("bw")
    here = lax.axis_index(SPREAD)
    widths = jnp.concatenate([inverse_width, swap_cores(inverse_width)])
    weights = jnp.concatenate([mixture, swap_cores(mixture)])
    count = lax.axis_size(SPREAD)
    chosen = normalize(lax.dynamic_slice_in_dim(candidates, core * half, half, axis=0))
    chosen, widths, weights = lax.optimization_barrier((chosen, widths, weights))
    pieces = chosen.reshape(count, half // count, chosen.shape[1])
    spread = lax.all_to_all(pieces, SPREAD, 0, 0, tiled=True)
    kept = jnp.stack(
        [
            lax.dynamic_index_in_dim(spread, block_owner[number], 0, keepdims=False)
            for number in range(block_count)
        ]
    )
    arrived = [
        lax.all_to_all(
            jnp.broadcast_to(kept[number][None], (count,) + kept.shape[1:]), SPREAD, 0, 0, tiled=True
        ).reshape(half, chosen.shape[1])
        for number in range(block_count)
    ]
    share = unit_rows.shape[0] // cores
    own_rows = lax.dynamic_slice_in_dim(unit_rows, core * share, share, axis=0)
    own_features = jnp.zeros((share, whitening.shape[1]), jnp.float32)
    other_features = jnp.zeros((share, whitening.shape[1]), jnp.float32)
    for number in range(block_count):
        mine = arrived[number]
        if number > 0:
            mine, own_features, other_features = lax.optimization_barrier(
                (mine, own_features, other_features)
            )
        other = swap_cores(mine)
        parts = [
            kernel_of(inner_products(own_rows, landmark), widths, weights).astype(jnp.bfloat16)
            for landmark in (mine, other)
        ]
        own_kernel = jnp.where(
            core == 0,
            jnp.concatenate(parts, axis=1),
            jnp.concatenate(parts[::-1], axis=1),
        )
        own_kernel = reorder_columns(own_kernel, landmark_picks[number])
        other_kernel = swap_cores(own_kernel)
        rows = lax.dynamic_slice_in_dim(whitening, number * block_rows, block_rows, axis=0)
        own_features = own_features + jnp.dot(own_kernel, rows, preferred_element_type=jnp.float32)
        other_features = other_features + jnp.dot(
            other_kernel, rows, preferred_element_type=jnp.float32
        )
    features = jnp.where(
        core == 0,
        jnp.concatenate([own_features, other_features], axis=0),
        jnp.concatenate([other_features, own_features], axis=0),
    )
    return features.astype(jnp.bfloat16)


def solution(mesh):
    in_specs = (
        P(SPREAD, None),
        P(SPREAD, None),
        P(),
        P(),
        P("bw"),
        P("bw"),
        P(None, "bw"),
    )
    out_specs = P(SPREAD, "bw")
    return jax.shard_map(
        per_device, mesh=mesh, in_specs=in_specs, out_specs=out_specs, check_vma=False
    )
```

```python
import jax
import jax.numpy as jnp
from jax import lax
from jax.sharding import PartitionSpec as P

SPREAD = ("row", "lmk")


def normalize(matrix_rows):
    widened = matrix_rows.astype(jnp.float32)
    scale = lax.rsqrt(jnp.sum(widened * widened, axis=-1, keepdims=True) + 1e-06)
    return (widened * scale).astype(jnp.bfloat16)


def kernel_of(cosine, widths, weights):
    running = jnp.zeros(cosine.shape, jnp.float32)
    for which in range(widths.shape[0]):
        running = running + weights[which] * jnp.exp(2.0 * widths[which] * cosine)
    return running


def inner_products(unit_rows, landmark):
    return jnp.einsum("rd,md->rm", unit_rows, landmark, preferred_element_type=jnp.float32)


def reorder_columns(kernel, picks):
    natural = lax.broadcasted_iota(jnp.int32, (kernel.shape[1], picks.shape[0]), 0)
    onehot = (picks[None, :] == natural).astype(kernel.dtype)
    ordered = jnp.dot(kernel, onehot, preferred_element_type=jnp.float32)
    return ordered.astype(kernel.dtype)


def swap_cores(value):
    return lax.ppermute(value, "bw", [(0, 1), (1, 0)])


def per_device(
    embeddings, candidates, block_owner, landmark_picks, inverse_width, mixture, whitening
):
    own_rows = normalize(embeddings)
    block_count, block_rows = landmark_picks.shape
    cores = lax.axis_size("bw")
    half = block_rows // cores
    core = lax.axis_index("bw")
    here = lax.axis_index(SPREAD)
    widths = jnp.concatenate([inverse_width, swap_cores(inverse_width)])
    weights = jnp.concatenate([mixture, swap_cores(mixture)])
    count = lax.axis_size(SPREAD)
    chosen = candidates
    pieces = chosen.reshape(count, half // count, chosen.shape[1])
    spread = lax.all_to_all(pieces, SPREAD, 0, 0, tiled=True)
    kept = jnp.stack(
        [
            normalize(lax.dynamic_index_in_dim(spread, block_owner[number], 0, keepdims=False))
            for number in range(block_count)
        ]
    )
    kept, widths, weights = lax.optimization_barrier((kept, widths, weights))
    arrived = [
        lax.all_to_all(
            jnp.broadcast_to(kept[number][None], (count,) + kept.shape[1:]), SPREAD, 0, 0, tiled=True
        ).reshape(half, chosen.shape[1])
        for number in range(block_count)
    ]
    share = own_rows.shape[0]
    own_features = jnp.zeros((share, whitening.shape[1]), jnp.float32)
    other_features = jnp.zeros((share, whitening.shape[1]), jnp.float32)
    for number in range(block_count):
        mine = arrived[number]
        if number > 0:
            mine, own_features, other_features = lax.optimization_barrier(
                (mine, own_features, other_features)
            )
        other = swap_cores(mine)
        parts = [
            kernel_of(inner_products(own_rows, landmark), widths, weights).astype(jnp.bfloat16)
            for landmark in (mine, other)
        ]
        own_kernel = jnp.where(
            core == 0,
            jnp.concatenate(parts, axis=1),
            jnp.concatenate(parts[::-1], axis=1),
        )
        own_kernel = reorder_columns(own_kernel, landmark_picks[number])
        other_kernel = swap_cores(own_kernel)
        rows = lax.dynamic_slice_in_dim(whitening, number * block_rows, block_rows, axis=0)
        own_features = own_features + jnp.dot(own_kernel, rows, preferred_element_type=jnp.float32)
        other_features = other_features + jnp.dot(
            other_kernel, rows, preferred_element_type=jnp.float32
        )
    features = jnp.where(
        core == 0,
        jnp.concatenate([own_features, other_features], axis=0),
        jnp.concatenate([other_features, own_features], axis=0),
    )
    return features.astype(jnp.bfloat16)


def solution(mesh):
    in_specs = (
        P(SPREAD + ("bw",), None),
        P(SPREAD + ("bw",), None),
        P(),
        P(),
        P("bw"),
        P("bw"),
        P(None, "bw"),
    )
    out_specs = P(SPREAD, "bw")
    return jax.shard_map(
        per_device, mesh=mesh, in_specs=in_specs, out_specs=out_specs, check_vma=False
    )
```

```python
import jax
import jax.numpy as jnp
from jax import lax
from jax.sharding import PartitionSpec as P

SPREAD = ("row", "lmk")


def normalize(matrix_rows):
    widened = matrix_rows.astype(jnp.float32)
    scale = lax.rsqrt(jnp.sum(widened * widened, axis=-1, keepdims=True) + 1e-06)
    return (widened * scale).astype(jnp.bfloat16)


def kernel_of(cosine, widths, weights):
    running = jnp.zeros(cosine.shape, jnp.float32)
    for which in range(widths.shape[0]):
        running = running + weights[which] * jnp.exp(2.0 * widths[which] * cosine)
    return running


def inner_products(unit_rows, landmark):
    return jnp.einsum("rd,md->rm", unit_rows, landmark, preferred_element_type=jnp.float32)


def reorder_columns(kernel, picks):
    natural = lax.broadcasted_iota(jnp.int32, (kernel.shape[1], picks.shape[0]), 0)
    onehot = (picks[None, :] == natural).astype(kernel.dtype)
    ordered = jnp.dot(kernel, onehot, preferred_element_type=jnp.float32)
    return ordered.astype(kernel.dtype)


def swap_cores(value):
    return lax.ppermute(value, "bw", [(0, 1), (1, 0)])


def per_device(
    embeddings, candidates, block_owner, landmark_picks, inverse_width, mixture, whitening
):
    own_rows = normalize(embeddings)
    block_count, block_rows = landmark_picks.shape
    cores = lax.axis_size("bw")
    half = block_rows // cores
    core = lax.axis_index("bw")
    here = lax.axis_index(SPREAD)
    widths = jnp.concatenate([inverse_width, swap_cores(inverse_width)])
    weights = jnp.concatenate([mixture, swap_cores(mixture)])
    count = lax.axis_size(SPREAD)
    chosen = candidates
    pieces = chosen.reshape(count, half // count, chosen.shape[1])
    spread = lax.all_to_all(pieces, SPREAD, 0, 0, tiled=True)
    kept = jnp.stack(
        [
            normalize(lax.dynamic_index_in_dim(spread, block_owner[number], 0, keepdims=False))
            for number in range(block_count)
        ]
    )
    kept, widths, weights = lax.optimization_barrier((kept, widths, weights))
    arrived = [
        lax.all_to_all(
            jnp.broadcast_to(kept[number][None], (count,) + kept.shape[1:]), SPREAD, 0, 0, tiled=True
        ).reshape(half, chosen.shape[1])
        for number in range(block_count)
    ]
    share = own_rows.shape[0]
    own_features = jnp.zeros((share, whitening.shape[1]), jnp.float32)
    other_features = jnp.zeros((share, whitening.shape[1]), jnp.float32)
    for number in range(block_count):
        mine = arrived[number]
        if number > 0:
            mine, own_features, other_features = lax.optimization_barrier(
                (mine, own_features, other_features)
            )
        other = swap_cores(mine)
        parts = [
            kernel_of(inner_products(own_rows, landmark), widths, weights).astype(jnp.bfloat16)
            for landmark in (mine, other)
        ]
        own_kernel = jnp.where(
            core == 0,
            jnp.concatenate(parts, axis=1),
            jnp.concatenate(parts[::-1], axis=1),
        )
        own_kernel = reorder_columns(own_kernel, landmark_picks[number])
        other_kernel = swap_cores(own_kernel)
        rows = lax.dynamic_slice_in_dim(whitening, number * block_rows, block_rows, axis=0)
        own_features = own_features + jnp.dot(own_kernel, rows, preferred_element_type=jnp.float32)
        other_features = other_features + jnp.dot(
            other_kernel, rows, preferred_element_type=jnp.float32
        )
    features = jnp.zeros((cores * share, whitening.shape[1]), jnp.bfloat16)
    features = lax.dynamic_update_slice_in_dim(
        features, own_features.astype(jnp.bfloat16), core * share, axis=0
    )
    return lax.dynamic_update_slice_in_dim(
        features, other_features.astype(jnp.bfloat16), (1 - core) * share, axis=0
    )


def solution(mesh):
    in_specs = (
        P(SPREAD + ("bw",), None),
        P(SPREAD + ("bw",), None),
        P(),
        P(),
        P("bw"),
        P("bw"),
        P(None, "bw"),
    )
    out_specs = P(SPREAD, "bw")
    return jax.shard_map(
        per_device, mesh=mesh, in_specs=in_specs, out_specs=out_specs, check_vma=False
    )
```
